256 devices in a mesh: dp: 4 (over z_lo), frame: 16 (over x, y), row: 4 (over z_hi, core).
Axes of the slice: x: 4, y: 4, z: 8 (z_hi: 2, z_lo: 4; z = z_hi * 4 + z_lo), core: 2. Of those that a mesh axis runs over, the one named last changes fastest.
Arguments:
- clip_input: bfloat16 [4, 64, 16, 240, 128], P('dp', 'frame', 'row'), may hold values from -6 to 6
- cotangent: bfloat16 [4, 64, 16, 240, 128], P('dp', 'frame', 'row'), may hold values from -6 to 6
- spatial_weight: bfloat16 [3, 3, 128, 128], replicated, may hold values from -0.1875 to 0.1875
- temporal_weight: bfloat16 [3, 128, 128], replicated, may hold values from -0.3125 to 0.3125
Outputs:
- block_output: bfloat16 [4, 64, 16, 240, 128], P('dp', 'frame', 'row')
- input_grad: bfloat16 [4, 64, 16, 240, 128], P('dp', 'frame', 'row')
- weight_grads: float32 [1536, 128], P(('dp', 'frame', 'row'))
The draws below stay inside these ranges and needn't reach their ends.
All inputs are finite; a program needn't handle non-finite values.
Results may differ from the reference program's by a relative error of at most 0.0045.
Values may be sent and summed in bfloat16 or wider, within the bound.
No kernel may reach another device: no remote copies, remote signals or barrier semaphores. Data moves between devices by JAX's collectives and lax.ppermute only.
A program may use at most 64 MiB of HBM per device.

```python
import math
import jax
import jax.numpy as jnp
from jax import lax

C = 128
W = 240
CLIPS = 4
FRAMES = 64
H = 16
CELLS = 983040


def block_levels(rng, dims, shards, smallest, top_value):
    loudness = 1.0
    for position, shards_of in shards:
        steps = jax.random.uniform(jax.random.fold_in(jax.random.fold_in(rng, 6), position), (shards_of,), jnp.float32, smallest / len(shards), top_value / len(shards))
        loudness = loudness * jnp.repeat(jnp.exp(steps), dims[position] // shards_of).reshape((-1,) + (1,) * (len(dims) - 1 - position))
    return loudness


def noise(key, shape, width, most, pieces=(), held_as=jnp.bfloat16):
    entries = jax.random.normal(key, shape, jnp.float32) * width
    if len(pieces) > 0:
        entries = block_levels(key, shape, pieces, -0.22, 0.18) * entries
    return jnp.clip(entries, min=-most, max=most).astype(held_as)


def setup_inputs(seed: int = 0) -> dict:
    streams_of = jax.random.split(jax.random.key(seed), 5)
    clip_input = noise(streams_of[0], (CLIPS, FRAMES, H, W, C), 1.0, 6.0, ((0, 4), (1, 16), (2, 4)))
    cotangent = noise(streams_of[1], (CLIPS, FRAMES, H, W, C), 1.0, 6.0, ((0, 4), (1, 16), (2, 4)))
    spatial_weight = noise(streams_of[2], (3, 3, C, C), (9 * C) ** -0.5, 0.1875)
    temporal_weight = noise(streams_of[3], (3, C, C), (3 * C) ** -0.5, 0.3125)
    return dict(clip_input=clip_input, cotangent=cotangent, spatial_weight=spatial_weight, temporal_weight=temporal_weight)


def spatial_taps(padded, weights, rows, cols):
    chans = padded.shape[-1]
    total = jnp.zeros((padded.shape[0] * rows * cols, weights.shape[-1]), jnp.float32)
    for i in range(3):
        for j in range(3):
            piece = padded[:, i:i + rows, j:j + cols, :].reshape(-1, chans)
            total = total + jnp.dot(piece, weights[i, j], preferred_element_type=jnp.float32)
    return total.reshape(padded.shape[0], rows, cols, -1)

def contract_rows(left, right):
    return lax.dot_general(left, right, (((0,), (0,)), ((), ())), preferred_element_type=jnp.float32)

def clip_pass(clip_x, clip_g, spatial_weight, temporal_weight):
    frames, rows, cols, chans = clip_x.shape
    xpad = jnp.pad(clip_x, ((0, 0), (1, 1), (1, 1), (0, 0)))
    pre = spatial_taps(xpad, spatial_weight, rows, cols)
    act = jax.nn.silu(pre).astype(jnp.bfloat16)
    act_ext = jnp.pad(act, ((2, 0), (0, 0), (0, 0), (0, 0)))
    grad_ext = jnp.pad(clip_g, ((0, 2), (0, 0), (0, 0), (0, 0)))
    mixed = jnp.zeros((frames * rows * cols, chans), jnp.float32)
    act_grad = jnp.zeros((frames * rows * cols, chans), jnp.float32)
    g_flat = clip_g.reshape(-1, chans)
    temporal_list = []
    for k in range(3):
        shifted = act_ext[2 - k:2 - k + frames].reshape(-1, chans)
        mixed = mixed + jnp.dot(shifted, temporal_weight[k], preferred_element_type=jnp.float32)
        later = grad_ext[k:k + frames].reshape(-1, chans)
        act_grad = act_grad + jnp.dot(later, temporal_weight[k].T, preferred_element_type=jnp.float32)
        temporal_list.append(contract_rows(shifted, g_flat))
    mixed = mixed.astype(jnp.bfloat16).reshape(clip_x.shape)
    block_output = (clip_x.astype(jnp.float32) + mixed.astype(jnp.float32)).astype(jnp.bfloat16)
    act_grad = act_grad.astype(jnp.bfloat16).reshape(clip_x.shape)
    sig = jax.nn.sigmoid(pre)
    pre_grad = (act_grad.astype(jnp.float32) * sig * (1.0 + pre * (1.0 - sig))).astype(jnp.bfloat16)
    pg_flat = pre_grad.reshape(-1, chans)
    spatial_list = []
    for i in range(3):
        for j in range(3):
            piece = xpad[:, i:i + rows, j:j + cols, :].reshape(-1, chans)
            spatial_list.append(contract_rows(piece, pg_flat))
    gpad = jnp.pad(pre_grad, ((0, 0), (1, 1), (1, 1), (0, 0)))
    back = jnp.zeros((frames * rows * cols, chans), jnp.float32)
    for i in range(3):
        for j in range(3):
            piece = gpad[:, 2 - i:2 - i + rows, 2 - j:2 - j + cols, :].reshape(-1, chans)
            back = back + jnp.dot(piece, spatial_weight[i, j].T, preferred_element_type=jnp.float32)
    input_grad = (clip_g.astype(jnp.float32).reshape(-1, chans) + back).astype(jnp.bfloat16).reshape(clip_x.shape)
    grads = jnp.concatenate(spatial_list + temporal_list, axis=0)
    return (block_output, input_grad, grads)

def reference(clip_input, cotangent, spatial_weight, temporal_weight):

    def one_clip(pair):
        return clip_pass(pair[0], pair[1], spatial_weight, temporal_weight)
    outputs, grads_in, grads = lax.map(one_clip, (clip_input, cotangent))
    weight_grads = lax.optimization_barrier(jnp.sum(grads, axis=0)) * (1.0 / math.sqrt(CELLS))
    return (outputs, grads_in, weight_grads)
```

```python
import math

import jax
import jax.numpy as jnp
from jax import lax
from jax.sharding import PartitionSpec as P


def extended_2(shard, sides, width):
    for axis, dim in sides:
        peers, length = (lax.axis_size(axis), shard.shape[dim])
        up = [(i, (i + 1) % peers) for i in range(peers - 1)]
        down = [(j, i) for i, j in up]
        last = lax.slice_in_dim(shard, length - width, length, axis=dim)
        first = lax.slice_in_dim(shard, 0, width, axis=dim)
        before = lax.ppermute(last, axis, up)
        after = lax.ppermute(first, axis, down)
        shard = jnp.concatenate([before, shard, after], axis=dim)
    return shard


def spatial_taps(padded, weights, rows, cols):
    chans = padded.shape[-1]
    total = jnp.zeros((padded.shape[0] * rows * cols, weights.shape[-1]), jnp.float32)
    for i in range(3):
        for j in range(3):
            piece = padded[:, i : i + rows, j : j + cols, :].reshape(-1, chans)
            total = total + jnp.dot(piece, weights[i, j], preferred_element_type=jnp.float32)
    return total.reshape(padded.shape[0], rows, cols, -1)


def contract_rows(left, right):
    return lax.dot_general(
        left, right, (((0,), (0,)), ((), ())), preferred_element_type=jnp.float32
    )


def temporal_pass(earlier, act_now, grad_now, later, temporal_weight):
    frames = act_now.shape[0]
    chans = act_now.shape[-1]
    act_ext = jnp.concatenate([earlier, act_now], axis=0)
    grad_ext = jnp.concatenate([grad_now, later], axis=0)
    grad_flat = grad_now.reshape(-1, chans)
    mixed = jnp.zeros((grad_flat.shape[0], chans), jnp.float32)
    act_grad = jnp.zeros((grad_flat.shape[0], chans), jnp.float32)
    temporal_list = []
    for k in range(3):
        shifted = act_ext[2 - k : 2 - k + frames].reshape(-1, chans)
        mixed = mixed + jnp.dot(shifted, temporal_weight[k], preferred_element_type=jnp.float32)
        ahead = grad_ext[k : k + frames].reshape(-1, chans)
        act_grad = act_grad + jnp.dot(
            ahead, temporal_weight[k].T, preferred_element_type=jnp.float32
        )
        temporal_list.append(contract_rows(shifted, grad_flat))
    mixed = mixed.astype(jnp.bfloat16).reshape(act_now.shape)
    act_grad = act_grad.astype(jnp.bfloat16).reshape(act_now.shape)
    return (mixed, act_grad, jnp.concatenate(temporal_list, axis=0))


def staged_scatter(terms):
    n_dp, n_frame, n_row = (lax.axis_size(a) for a in ("dp", "frame", "row"))
    rows = terms.shape[0] // (n_dp * n_frame * n_row)
    blocks = terms.reshape(n_dp, n_frame, n_row, rows, terms.shape[-1])
    blocks = jnp.transpose(blocks, (2, 0, 1, 3, 4))
    blocks = lax.psum_scatter(blocks, "row", scatter_dimension=0, tiled=False)
    blocks = jnp.transpose(blocks, (1, 0, 2, 3))
    blocks = lax.psum_scatter(blocks, "frame", scatter_dimension=0, tiled=False)
    return lax.psum_scatter(blocks, "dp", scatter_dimension=0, tiled=False)


def on_device(clip_input, cotangent, spatial_weight, temporal_weight):
    frames = clip_input.shape[1]
    rows = clip_input.shape[2]
    cols = clip_input.shape[3]
    chans = clip_input.shape[4]
    cells = (
        lax.axis_size("dp") * frames * lax.axis_size("frame") * rows * lax.axis_size("row") * cols
    )
    scale = 1.0 / math.sqrt(cells)
    extended = extended_2(clip_input, (("row", 2),), 1)[0]
    xpad = jnp.pad(extended, ((0, 0), (0, 0), (1, 1), (0, 0)))
    pre = spatial_taps(xpad, spatial_weight, rows, cols)
    act = jax.nn.silu(pre).astype(jnp.bfloat16)
    grad_out = cotangent[0]
    act_band, grad_band = (
        lax.all_to_all(act[None], "frame", split_axis=3, concat_axis=1, tiled=True),
        lax.all_to_all(grad_out[None], "frame", split_axis=3, concat_axis=1, tiled=True),
    )
    act_band = act_band[0]
    grad_band = grad_band[0]
    edge_shape = (2,) + act_band.shape[1:]
    earlier = jnp.zeros(edge_shape, jnp.bfloat16)
    later = jnp.zeros(edge_shape, jnp.bfloat16)
    mixed_band, grad_act_band, temporal_terms = temporal_pass(
        earlier, act_band, grad_band, later, temporal_weight
    )
    mixed, act_grad = (
        lax.all_to_all(mixed_band[None], "frame", split_axis=1, concat_axis=3, tiled=True),
        lax.all_to_all(grad_act_band[None], "frame", split_axis=1, concat_axis=3, tiled=True),
    )
    mixed = mixed[0]
    act_grad = act_grad[0]
    block_output = (clip_input[0].astype(jnp.float32) + mixed.astype(jnp.float32)).astype(
        jnp.bfloat16
    )
    sigma = jax.nn.sigmoid(pre)
    pre_grad = (act_grad.astype(jnp.float32) * sigma * (1.0 + pre * (1.0 - sigma))).astype(
        jnp.bfloat16
    )
    pg_flat = pre_grad.reshape(-1, chans)
    spatial_list = []
    for i in range(3):
        for j in range(3):
            piece = xpad[:, i : i + rows, j : j + cols, :].reshape(-1, chans)
            spatial_list.append(contract_rows(piece, pg_flat))
    grad_ext = extended_2(pre_grad[None], (("row", 2),), 1)[0]
    gpad = jnp.pad(grad_ext, ((0, 0), (0, 0), (1, 1), (0, 0)))
    backward = jnp.zeros((frames * rows * cols, chans), jnp.float32)
    for i in range(3):
        for j in range(3):
            piece = gpad[:, 2 - i : 2 - i + rows, 2 - j : 2 - j + cols, :].reshape(-1, chans)
            backward = backward + jnp.dot(
                piece, spatial_weight[i, j].T, preferred_element_type=jnp.float32
            )
    input_grad = (grad_out.astype(jnp.float32).reshape(-1, chans) + backward).astype(jnp.bfloat16)
    input_grad = input_grad.reshape(clip_input.shape)
    partial_terms = jnp.concatenate(spatial_list + [temporal_terms], axis=0)
    summed = staged_scatter(partial_terms)
    return (block_output[None], input_grad, summed * scale)


def solution(mesh):
    placed = (P("dp", "frame", "row", None, None), P("dp", "frame", "row", None, None), P(), P())
    return jax.shard_map(
        on_device,
        mesh=mesh,
        in_specs=placed,
        out_specs=(
            P("dp", "frame", "row", None, None),
            P("dp", "frame", "row", None, None),
            P(("dp", "frame", "row"), None),
        ),
        check_vma=False,
    )
```

```python
import math

import jax
import jax.numpy as jnp
from jax import lax
from jax.sharding import PartitionSpec as P

CONV_DIMS = ("NHWC", "HWIO", "NHWC")
KERNEL_GRAD_DIMS = ("CHWN", "IHWO", "HWNC")


def row_halo(shard):
    peers = lax.axis_size("row")
    up = [(i, i + 1) for i in range(peers - 1)]
    down = [(i + 1, i) for i in range(peers - 1)]
    before = lax.ppermute(shard[:, -1:], "row", up)
    after = lax.ppermute(shard[:, :1], "row", down)
    return jnp.concatenate([before, shard, after], axis=1)


def frame_shift(piece, forward):
    peers = lax.axis_size("frame")
    if forward:
        pairs = [(i, i + 1) for i in range(peers - 1)]
    else:
        pairs = [(i + 1, i) for i in range(peers - 1)]
    return lax.ppermute(piece, "frame", pairs)


def a2a_sum(blocks, axis):
    got = lax.all_to_all(blocks, axis, split_axis=0, concat_axis=0, tiled=True)
    return jnp.sum(got, axis=0)


def staged_scatter(terms):
    n_dp, n_frame, n_row = (lax.axis_size(a) for a in ("dp", "frame", "row"))
    rows = terms.shape[0] // (n_dp * n_frame * n_row)
    chans = terms.shape[-1]
    blocks = terms.reshape(n_dp, n_frame, n_row, rows, chans)
    blocks = jnp.transpose(blocks, (2, 0, 1, 3, 4))
    blocks = a2a_sum(blocks, "row")
    blocks = jnp.transpose(blocks, (1, 0, 2, 3))
    blocks = a2a_sum(blocks, "frame")
    return a2a_sum(blocks, "dp")


def on_device(clip_input, cotangent, spatial_weight, temporal_weight):
    x = clip_input[0]
    g = cotangent[0]
    frames, rows, cols, chans = x.shape
    cells = (
        lax.axis_size("dp") * frames * lax.axis_size("frame") * rows * lax.axis_size("row") * cols
    )
    scale = 1.0 / math.sqrt(cells)
    f32 = jnp.float32

    x_ext = row_halo(x)
    g_next = frame_shift(g[:2], forward=False)
    pre = lax.conv_general_dilated(
        x_ext, spatial_weight, (1, 1), ((0, 0), (1, 1)),
        dimension_numbers=CONV_DIMS, preferred_element_type=f32,
    )
    act = jax.nn.silu(pre).astype(jnp.bfloat16)
    act_prev = frame_shift(act[frames - 2 :], forward=True)
    act_ext = jnp.concatenate([act_prev, act], axis=0)
    g_ext = jnp.concatenate([g, g_next], axis=0)
    g_flat = g.reshape(-1, chans)

    mixed = jnp.zeros((frames * rows * cols, chans), f32)
    act_grad = jnp.zeros((frames * rows * cols, chans), f32)
    temporal_list = []
    for k in range(3):
        shifted = act_ext[2 - k : 2 - k + frames].reshape(-1, chans)
        mixed = mixed + jnp.dot(shifted, temporal_weight[k], preferred_element_type=f32)
        ahead = g_ext[k : k + frames].reshape(-1, chans)
        act_grad = act_grad + jnp.dot(ahead, temporal_weight[k].T, preferred_element_type=f32)
        temporal_list.append(
            lax.dot_general(shifted, g_flat, (((0,), (0,)), ((), ())), preferred_element_type=f32)
        )
    mixed = mixed.astype(jnp.bfloat16).reshape(x.shape)
    act_grad = act_grad.astype(jnp.bfloat16).reshape(x.shape)
    block_output = (x.astype(f32) + mixed.astype(f32)).astype(jnp.bfloat16)

    sigma = jax.nn.sigmoid(pre)
    pre_grad = (act_grad.astype(f32) * sigma * (1.0 + pre * (1.0 - sigma))).astype(jnp.bfloat16)

    xpad = jnp.pad(x_ext, ((0, 0), (0, 0), (1, 1), (0, 0)))
    spatial_grad = lax.conv_general_dilated(
        xpad, pre_grad, (1, 1), ((0, 0), (0, 0)),
        dimension_numbers=KERNEL_GRAD_DIMS, preferred_element_type=f32,
    )
    pg_ext = row_halo(pre_grad)
    back_weight = jnp.transpose(jnp.flip(spatial_weight, (0, 1)), (0, 1, 3, 2))
    back = lax.conv_general_dilated(
        pg_ext, back_weight, (1, 1), ((0, 0), (1, 1)),
        dimension_numbers=CONV_DIMS, preferred_element_type=f32,
    )
    input_grad = (g.astype(f32) + back).astype(jnp.bfloat16)

    partial_terms = jnp.concatenate(
        [spatial_grad.reshape(-1, chans)] + temporal_list, axis=0
    )
    summed = staged_scatter(partial_terms)
    return (block_output[None], input_grad[None], summed * scale)


def solution(mesh):
    placed = (P("dp", "frame", "row", None, None), P("dp", "frame", "row", None, None), P(), P())
    return jax.shard_map(
        on_device,
        mesh=mesh,
        in_specs=placed,
        out_specs=(
            P("dp", "frame", "row", None, None),
            P("dp", "frame", "row", None, None),
            P(("dp", "frame", "row"), None),
        ),
        check_vma=False,
    )
```

```python
import math

import jax
import jax.numpy as jnp
from jax import lax
from jax.sharding import PartitionSpec as P


def row_halo(shard):
    peers = lax.axis_size("row")
    up = [(i, i + 1) for i in range(peers - 1)]
    down = [(i + 1, i) for i in range(peers - 1)]
    before = lax.ppermute(shard[:, -1:], "row", up)
    after = lax.ppermute(shard[:, :1], "row", down)
    return jnp.concatenate([before, shard, after], axis=1)


def frame_shift(piece, forward):
    peers = lax.axis_size("frame")
    if forward:
        pairs = [(i, i + 1) for i in range(peers - 1)]
    else:
        pairs = [(i + 1, i) for i in range(peers - 1)]
    return lax.ppermute(piece, "frame", pairs)


def a2a_sum(blocks, axis):
    got = lax.all_to_all(blocks, axis, split_axis=0, concat_axis=0, tiled=True)
    return jnp.sum(got, axis=0)


def staged_scatter(terms):
    n_dp, n_frame, n_row = (lax.axis_size(a) for a in ("dp", "frame", "row"))
    rows = terms.shape[0] // (n_dp * n_frame * n_row)
    chans = terms.shape[-1]
    blocks = terms.reshape(n_dp, n_frame, n_row, rows, chans)
    blocks = jnp.transpose(blocks, (2, 0, 1, 3, 4))
    blocks = a2a_sum(blocks, "row")
    blocks = jnp.transpose(blocks, (1, 0, 2, 3))
    blocks = a2a_sum(blocks, "frame")
    return a2a_sum(blocks, "dp")


def width_taps(a, reverse):
    zero = jnp.zeros_like(a[:, :, :1])
    left = jnp.concatenate([zero, a[:, :, :-1]], axis=2)
    right = jnp.concatenate([a[:, :, 1:], zero], axis=2)
    parts = [right, a, left] if reverse else [left, a, right]
    return jnp.concatenate(parts, axis=-1)


def on_device(clip_input, cotangent, spatial_weight, temporal_weight):
    x = clip_input[0]
    g = cotangent[0]
    frames, rows, cols, chans = x.shape
    cells = (
        lax.axis_size("dp") * frames * lax.axis_size("frame") * rows * lax.axis_size("row") * cols
    )
    scale = 1.0 / math.sqrt(cells)
    f32 = jnp.float32

    x_ext = row_halo(x)
    g_next = frame_shift(g[:2], forward=False)
    x3 = width_taps(x_ext, reverse=False)
    fwd_weight = spatial_weight.reshape(3, 3 * chans, chans)
    pre = jnp.zeros((frames * rows * cols, chans), f32)
    for i in range(3):
        piece = x3[:, i : i + rows].reshape(-1, 3 * chans)
        pre = pre + jnp.dot(piece, fwd_weight[i], preferred_element_type=f32)
    pre = pre.reshape(x.shape)
    act = jax.nn.silu(pre).astype(jnp.bfloat16)
    act_prev = frame_shift(act[frames - 2 :], forward=True)
    act_ext = jnp.concatenate([act_prev, act], axis=0)
    g_ext = jnp.concatenate([g, g_next], axis=0)
    g_flat = g.reshape(-1, chans)

    mixed = jnp.zeros((frames * rows * cols, chans), f32)
    act_grad = jnp.zeros((frames * rows * cols, chans), f32)
    temporal_list = []
    for k in range(3):
        shifted = act_ext[2 - k : 2 - k + frames].reshape(-1, chans)
        mixed = mixed + jnp.dot(shifted, temporal_weight[k], preferred_element_type=f32)
        ahead = g_ext[k : k + frames].reshape(-1, chans)
        act_grad = act_grad + jnp.dot(ahead, temporal_weight[k].T, preferred_element_type=f32)
        temporal_list.append(
            lax.dot_general(shifted, g_flat, (((0,), (0,)), ((), ())), preferred_element_type=f32)
        )
    mixed = mixed.astype(jnp.bfloat16).reshape(x.shape)
    act_grad = act_grad.astype(jnp.bfloat16).reshape(x.shape)
    block_output = (x.astype(f32) + mixed.astype(f32)).astype(jnp.bfloat16)

    sigma = jax.nn.sigmoid(pre)
    pre_grad = (act_grad.astype(f32) * sigma * (1.0 + pre * (1.0 - sigma))).astype(jnp.bfloat16)
    pg_flat = pre_grad.reshape(-1, chans)

    spatial_list = []
    for i in range(3):
        piece = x3[:, i : i + rows].reshape(-1, 3 * chans)
        spatial_list.append(
            lax.dot_general(piece, pg_flat, (((0,), (0,)), ((), ())), preferred_element_type=f32)
        )
    pg3 = width_taps(row_halo(pre_grad), reverse=True)
    back_weight = jnp.transpose(spatial_weight, (0, 1, 3, 2)).reshape(3, 3 * chans, chans)
    back = g.astype(f32).reshape(-1, chans)
    for i in range(3):
        piece = pg3[:, 2 - i : 2 - i + rows].reshape(-1, 3 * chans)
        back = back + jnp.dot(piece, back_weight[i], preferred_element_type=f32)
    input_grad = back.astype(jnp.bfloat16).reshape(x.shape)

    partial_terms = jnp.concatenate(spatial_list + temporal_list, axis=0)
    summed = staged_scatter(partial_terms)
    return (block_output[None], input_grad[None], summed * scale)


def solution(mesh):
    placed = (P("dp", "frame", "row", None, None), P("dp", "frame", "row", None, None), P(), P())
    return jax.shard_map(
        on_device,
        mesh=mesh,
        in_specs=placed,
        out_specs=(
            P("dp", "frame", "row", None, None),
            P("dp", "frame", "row", None, None),
            P(("dp", "frame", "row"), None),
        ),
        check_vma=False,
    )
```

```python
import math

import jax
import jax.numpy as jnp
from jax import lax
from jax.sharding import PartitionSpec as P


def row_halo(shard, width):
    peers = lax.axis_size("row")
    up = [(i, i + 1) for i in range(peers - 1)]
    down = [(i + 1, i) for i in range(peers - 1)]
    before = lax.ppermute(shard[:, shard.shape[1] - width :], "row", up)
    after = lax.ppermute(shard[:, :width], "row", down)
    return jnp.concatenate([before, shard, after], axis=1)


def frame_shift(piece, forward):
    peers = lax.axis_size("frame")
    if forward:
        pairs = [(i, i + 1) for i in range(peers - 1)]
    else:
        pairs = [(i + 1, i) for i in range(peers - 1)]
    return lax.ppermute(piece, "frame", pairs)


def a2a_sum(blocks, axis):
    got = lax.all_to_all(blocks, axis, split_axis=0, concat_axis=0, tiled=True)
    return jnp.sum(got, axis=0)


def staged_scatter(terms):
    axes = ("dp", "frame", "row")
    n = 1
    for a in axes:
        n *= lax.axis_size(a)
    return a2a_sum(terms.reshape(n, terms.shape[0] // n, terms.shape[-1]), axes)


def width_taps(a, reverse):
    zero = jnp.zeros_like(a[:, :, :1])
    left = jnp.concatenate([zero, a[:, :, :-1]], axis=2)
    right = jnp.concatenate([a[:, :, 1:], zero], axis=2)
    parts = [right, a, left] if reverse else [left, a, right]
    return jnp.concatenate(parts, axis=-1)


def on_device(clip_input, cotangent, spatial_weight, temporal_weight):
    x = clip_input[0]
    g = cotangent[0]
    frames, rows, cols, chans = x.shape
    cells = (
        lax.axis_size("dp") * frames * lax.axis_size("frame") * rows * lax.axis_size("row") * cols
    )
    scale = 1.0 / math.sqrt(cells)
    f32 = jnp.float32

    x_f = jnp.concatenate([frame_shift(x[frames - 2 :], forward=True), x], axis=0)
    x_e = row_halo(x_f, 2)
    g_f = jnp.concatenate([g, frame_shift(g[:2], forward=False)], axis=0)
    g_e = row_halo(g_f, 1)

    x3 = width_taps(x_e, reverse=False)
    fwd_weight = spatial_weight.reshape(3, 3 * chans, chans)
    wide = (frames + 2, rows + 2, cols, chans)
    pre = jnp.zeros((math.prod(wide[:-1]), chans), f32)
    for i in range(3):
        piece = x3[:, i : i + rows + 2].reshape(-1, 3 * chans)
        pre = pre + jnp.dot(piece, fwd_weight[i], preferred_element_type=f32)
    pre = pre.reshape(wide)
    act = jax.nn.silu(pre[:, 1 : rows + 1]).astype(jnp.bfloat16)
    g_flat = g.reshape(-1, chans)

    mixed = jnp.zeros((frames * rows * cols, chans), f32)
    act_grad = jnp.zeros((frames * (rows + 2) * cols, chans), f32)
    temporal_list = []
    for k in range(3):
        shifted = act[2 - k : 2 - k + frames].reshape(-1, chans)
        mixed = mixed + jnp.dot(shifted, temporal_weight[k], preferred_element_type=f32)
        ahead = g_e[k : k + frames].reshape(-1, chans)
        act_grad = act_grad + jnp.dot(ahead, temporal_weight[k].T, preferred_element_type=f32)
        temporal_list.append(
            lax.dot_general(shifted, g_flat, (((0,), (0,)), ((), ())), preferred_element_type=f32)
        )
    mixed = mixed.astype(jnp.bfloat16).reshape(x.shape)
    act_grad = act_grad.astype(jnp.bfloat16).reshape(frames, rows + 2, cols, chans)
    block_output = (x.astype(f32) + mixed.astype(f32)).astype(jnp.bfloat16)

    pre_now = pre[2:]
    sigma = jax.nn.sigmoid(pre_now)
    pg_ext = (act_grad.astype(f32) * sigma * (1.0 + pre_now * (1.0 - sigma))).astype(jnp.bfloat16)
    pg_flat = pg_ext[:, 1 : rows + 1].reshape(-1, chans)

    spatial_list = []
    for i in range(3):
        piece = x3[2:, 1 + i : 1 + i + rows].reshape(-1, 3 * chans)
        spatial_list.append(
            lax.dot_general(piece, pg_flat, (((0,), (0,)), ((), ())), preferred_element_type=f32)
        )
    pg3 = width_taps(pg_ext, reverse=True)
    back_weight = jnp.transpose(spatial_weight, (0, 1, 3, 2)).reshape(3, 3 * chans, chans)
    back = g.astype(f32).reshape(-1, chans)
    for i in range(3):
        piece = pg3[:, 2 - i : 2 - i + rows].reshape(-1, 3 * chans)
        back = back + jnp.dot(piece, back_weight[i], preferred_element_type=f32)
    input_grad = back.astype(jnp.bfloat16).reshape(x.shape)

    partial_terms = jnp.concatenate(spatial_list + temporal_list, axis=0)
    summed = staged_scatter(partial_terms)
    return (block_output[None], input_grad[None], summed * scale)


def solution(mesh):
    placed = (P("dp", "frame", "row", None, None), P("dp", "frame", "row", None, None), P(), P())
    return jax.shard_map(
        on_device,
        mesh=mesh,
        in_specs=placed,
        out_specs=(
            P("dp", "frame", "row", None, None),
            P("dp", "frame", "row", None, None),
            P(("dp", "frame", "row"), None),
        ),
        check_vma=False,
    )
```

```python
import math

import jax
import jax.numpy as jnp
from jax import lax
from jax.sharding import PartitionSpec as P


def row_halo(shard, width):
    peers = lax.axis_size("row")
    up = [(i, i + 1) for i in range(peers - 1)]
    down = [(i + 1, i) for i in range(peers - 1)]
    before = lax.ppermute(shard[:, shard.shape[1] - width :], "row", up)
    after = lax.ppermute(shard[:, :width], "row", down)
    return jnp.concatenate([before, shard, after], axis=1)


def frame_shift(piece, forward):
    peers = lax.axis_size("frame")
    if forward:
        pairs = [(i, i + 1) for i in range(peers - 1)]
    else:
        pairs = [(i + 1, i) for i in range(peers - 1)]
    return lax.ppermute(piece, "frame", pairs)


def a2a_sum(blocks, axis):
    got = lax.all_to_all(blocks, axis, split_axis=0, concat_axis=0, tiled=True)
    return jnp.sum(got, axis=0)


def staged_scatter(terms):
    n_dp, n_frame, n_row = (lax.axis_size(a) for a in ("dp", "frame", "row"))
    rows = terms.shape[0] // (n_dp * n_frame * n_row)
    chans = terms.shape[-1]
    blocks = terms.reshape(n_dp, n_frame, n_row, rows, chans)
    blocks = jnp.transpose(blocks, (2, 0, 1, 3, 4))
    blocks = a2a_sum(blocks, "row")
    blocks = jnp.transpose(blocks, (1, 0, 2, 3))
    blocks = a2a_sum(blocks, "frame")
    return a2a_sum(blocks, "dp")


def width_taps(a, reverse):
    zero = jnp.zeros_like(a[:, :, :1])
    left = jnp.concatenate([zero, a[:, :, :-1]], axis=2)
    right = jnp.concatenate([a[:, :, 1:], zero], axis=2)
    parts = [right, a, left] if reverse else [left, a, right]
    return jnp.concatenate(parts, axis=-1)


def grid_shift(piece, df, dr):
    n_f, n_r = lax.axis_size("frame"), lax.axis_size("row")
    pairs = [
        (f * n_r + r, (f + df) * n_r + (r + dr))
        for f in range(n_f)
        for r in range(n_r)
        if 0 <= f + df < n_f and 0 <= r + dr < n_r
    ]
    return lax.ppermute(piece, ("frame", "row"), pairs)


def halos(x, g):
    frames, rows = x.shape[:2]
    down = grid_shift(jnp.concatenate([x[:, rows - 2 :], g[:, rows - 1 :]], axis=1), 0, 1)
    up = grid_shift(jnp.concatenate([x[:, :2], g[:, :1]], axis=1), 0, -1)
    x_mid = grid_shift(x[frames - 2 :], 1, 0)
    x_above = grid_shift(x[frames - 2 :, rows - 2 :], 1, 1)
    x_below = grid_shift(x[frames - 2 :, :2], 1, -1)
    g_mid = grid_shift(g[:2], -1, 0)
    g_above = grid_shift(g[:2, rows - 1 :], -1, 1)
    g_below = grid_shift(g[:2, :1], -1, -1)
    x_e = jnp.concatenate(
        [
            jnp.concatenate([x_above, x_mid, x_below], axis=1),
            jnp.concatenate([down[:, :2], x, up[:, :2]], axis=1),
        ],
        axis=0,
    )
    g_e = jnp.concatenate(
        [
            jnp.concatenate([down[:, 2:], g, up[:, 2:]], axis=1),
            jnp.concatenate([g_above, g_mid, g_below], axis=1),
        ],
        axis=0,
    )
    return x_e, g_e


def on_device(clip_input, cotangent, spatial_weight, temporal_weight):
    x = clip_input[0]
    g = cotangent[0]
    frames, rows, cols, chans = x.shape
    cells = (
        lax.axis_size("dp") * frames * lax.axis_size("frame") * rows * lax.axis_size("row") * cols
    )
    scale = 1.0 / math.sqrt(cells)
    f32 = jnp.float32

    x_e, g_e = halos(x, g)

    x3 = width_taps(x_e, reverse=False)
    fwd_weight = spatial_weight.reshape(3, 3 * chans, chans)
    wide = (frames + 2, rows + 2, cols, chans)
    pre = jnp.zeros((math.prod(wide[:-1]), chans), f32)
    for i in range(3):
        piece = x3[:, i : i + rows + 2].reshape(-1, 3 * chans)
        pre = pre + jnp.dot(piece, fwd_weight[i], preferred_element_type=f32)
    pre = pre.reshape(wide)
    act = jax.nn.silu(pre[:, 1 : rows + 1]).astype(jnp.bfloat16)
    g_flat = g.reshape(-1, chans)

    mixed = jnp.zeros((frames * rows * cols, chans), f32)
    act_grad = jnp.zeros((frames * (rows + 2) * cols, chans), f32)
    temporal_list = []
    for k in range(3):
        shifted = act[2 - k : 2 - k + frames].reshape(-1, chans)
        mixed = mixed + jnp.dot(shifted, temporal_weight[k], preferred_element_type=f32)
        ahead = g_e[k : k + frames].reshape(-1, chans)
        act_grad = act_grad + jnp.dot(ahead, temporal_weight[k].T, preferred_element_type=f32)
        temporal_list.append(
            lax.dot_general(shifted, g_flat, (((0,), (0,)), ((), ())), preferred_element_type=f32)
        )
    mixed = mixed.astype(jnp.bfloat16).reshape(x.shape)
    act_grad = act_grad.astype(jnp.bfloat16).reshape(frames, rows + 2, cols, chans)
    block_output = (x.astype(f32) + mixed.astype(f32)).astype(jnp.bfloat16)

    pre_now = pre[2:]
    sigma = jax.nn.sigmoid(pre_now)
    pg_ext = (act_grad.astype(f32) * sigma * (1.0 + pre_now * (1.0 - sigma))).astype(jnp.bfloat16)
    pg_flat = pg_ext[:, 1 : rows + 1].reshape(-1, chans)

    spatial_list = []
    for i in range(3):
        piece = x3[2:, 1 + i : 1 + i + rows].reshape(-1, 3 * chans)
        spatial_list.append(
            lax.dot_general(piece, pg_flat, (((0,), (0,)), ((), ())), preferred_element_type=f32)
        )
    pg3 = width_taps(pg_ext, reverse=True)
    back_weight = jnp.transpose(spatial_weight, (0, 1, 3, 2)).reshape(3, 3 * chans, chans)
    back = g.astype(f32).reshape(-1, chans)
    for i in range(3):
        piece = pg3[:, 2 - i : 2 - i + rows].reshape(-1, 3 * chans)
        back = back + jnp.dot(piece, back_weight[i], preferred_element_type=f32)
    input_grad = back.astype(jnp.bfloat16).reshape(x.shape)

    partial_terms = jnp.concatenate(spatial_list + temporal_list, axis=0)
    summed = staged_scatter(partial_terms)
    return (block_output[None], input_grad[None], summed * scale)


def solution(mesh):
    placed = (P("dp", "frame", "row", None, None), P("dp", "frame", "row", None, None), P(), P())
    return jax.shard_map(
        on_device,
        mesh=mesh,
        in_specs=placed,
        out_specs=(
            P("dp", "frame", "row", None, None),
            P("dp", "frame", "row", None, None),
            P(("dp", "frame", "row"), None),
        ),
        check_vma=False,
    )
```

```python
import math

import jax
import jax.numpy as jnp
from jax import lax
from jax.sharding import PartitionSpec as P


def row_halo(shard):
    peers = lax.axis_size("row")
    up = [(i, i + 1) for i in range(peers - 1)]
    down = [(i + 1, i) for i in range(peers - 1)]
    before = lax.ppermute(shard[-1:], "row", up)
    after = lax.ppermute(shard[:1], "row", down)
    return jnp.concatenate([before, shard, after], axis=0)


def frame_shift(piece, forward):
    peers = lax.axis_size("frame")
    if forward:
        pairs = [(i, i + 1) for i in range(peers - 1)]
    else:
        pairs = [(i + 1, i) for i in range(peers - 1)]
    return lax.ppermute(piece, "frame", pairs)


def a2a_sum(blocks, axis):
    got = lax.all_to_all(blocks, axis, split_axis=0, concat_axis=0, tiled=True)
    return jnp.sum(got, axis=0)


def staged_scatter(terms):
    n_dp, n_frame, n_row = (lax.axis_size(a) for a in ("dp", "frame", "row"))
    rows = terms.shape[0] // (n_dp * n_frame * n_row)
    chans = terms.shape[-1]
    blocks = terms.reshape(n_dp, n_frame, n_row, rows, chans)
    blocks = jnp.transpose(blocks, (2, 0, 1, 3, 4))
    blocks = a2a_sum(blocks, "row")
    blocks = jnp.transpose(blocks, (1, 0, 2, 3))
    blocks = a2a_sum(blocks, "frame")
    return a2a_sum(blocks, "dp")


def width_taps(a, reverse):
    zero = jnp.zeros_like(a[:, :, :1])
    left = jnp.concatenate([zero, a[:, :, :-1]], axis=2)
    right = jnp.concatenate([a[:, :, 1:], zero], axis=2)
    parts = [right, a, left] if reverse else [left, a, right]
    return jnp.concatenate(parts, axis=-1)


def frame_taps(ext, frames, later):
    if later:
        parts = [ext[:, k : k + frames] for k in range(3)]
    else:
        parts = [ext[:, 2 - k : 2 - k + frames] for k in range(3)]
    return jnp.concatenate(parts, axis=-1)


def on_device(clip_input, cotangent, spatial_weight, temporal_weight):
    x = jnp.transpose(clip_input[0], (1, 0, 2, 3))
    g = jnp.transpose(cotangent[0], (1, 0, 2, 3))
    rows, frames, cols, chans = x.shape
    cells = (
        lax.axis_size("dp") * frames * lax.axis_size("frame") * rows * lax.axis_size("row") * cols
    )
    scale = 1.0 / math.sqrt(cells)
    f32 = jnp.float32
    bf16 = jnp.bfloat16

    x_ext = row_halo(x)
    g_next = frame_shift(g[:, :2], forward=False)
    x3 = width_taps(x_ext, reverse=False)
    fwd_weight = spatial_weight.reshape(3, 3 * chans, chans)
    pre = jnp.zeros((rows * frames * cols, chans), f32)
    for i in range(3):
        piece = x3[i : i + rows].reshape(-1, 3 * chans)
        pre = pre + jnp.dot(piece, fwd_weight[i], preferred_element_type=f32)
    pre = pre.reshape(x.shape)
    act = jax.nn.silu(pre).astype(bf16)
    act_prev = frame_shift(act[:, frames - 2 :], forward=True)
    act3 = frame_taps(jnp.concatenate([act_prev, act], axis=1), frames, later=False)
    g3 = frame_taps(jnp.concatenate([g, g_next], axis=1), frames, later=True)
    act3_flat = act3.reshape(-1, 3 * chans)
    g_flat = g.reshape(-1, chans)

    mixed = jnp.dot(act3_flat, temporal_weight.reshape(3 * chans, chans), preferred_element_type=f32)
    back_temporal = jnp.transpose(temporal_weight, (0, 2, 1)).reshape(3 * chans, chans)
    act_grad = jnp.dot(g3.reshape(-1, 3 * chans), back_temporal, preferred_element_type=f32)
    temporal_grad = lax.dot_general(
        act3_flat, g_flat, (((0,), (0,)), ((), ())), preferred_element_type=f32
    )
    mixed = mixed.astype(bf16).reshape(x.shape)
    act_grad = act_grad.astype(bf16).reshape(x.shape)
    block_output = (x.astype(f32) + mixed.astype(f32)).astype(bf16)

    sigma = jax.nn.sigmoid(pre)
    pre_grad = (act_grad.astype(f32) * sigma * (1.0 + pre * (1.0 - sigma))).astype(bf16)
    pg_flat = pre_grad.reshape(-1, chans)

    spatial_list = []
    for i in range(3):
        piece = x3[i : i + rows].reshape(-1, 3 * chans)
        spatial_list.append(
            lax.dot_general(piece, pg_flat, (((0,), (0,)), ((), ())), preferred_element_type=f32)
        )
    pg3 = width_taps(row_halo(pre_grad), reverse=True)
    back_weight = jnp.transpose(spatial_weight, (0, 1, 3, 2)).reshape(3, 3 * chans, chans)
    back = g.astype(f32).reshape(-1, chans)
    for i in range(3):
        piece = pg3[2 - i : 2 - i + rows].reshape(-1, 3 * chans)
        back = back + jnp.dot(piece, back_weight[i], preferred_element_type=f32)
    input_grad = back.astype(bf16).reshape(x.shape)

    partial_terms = jnp.concatenate(spatial_list + [temporal_grad], axis=0)
    summed = staged_scatter(partial_terms)
    block_output = jnp.transpose(block_output, (1, 0, 2, 3))
    input_grad = jnp.transpose(input_grad, (1, 0, 2, 3))
    return (block_output[None], input_grad[None], summed * scale)


def solution(mesh):
    placed = (P("dp", "frame", "row", None, None), P("dp", "frame", "row", None, None), P(), P())
    return jax.shard_map(
        on_device,
        mesh=mesh,
        in_specs=placed,
        out_specs=(
            P("dp", "frame", "row", None, None),
            P("dp", "frame", "row", None, None),
            P(("dp", "frame", "row"), None),
        ),
        check_vma=False,
    )
```

```python
import math

import jax
import jax.numpy as jnp
from jax import lax
from jax.sharding import PartitionSpec as P


def row_halo(shard):
    peers = lax.axis_size("row")
    up = [(i, i + 1) for i in range(peers - 1)]
    down = [(i + 1, i) for i in range(peers - 1)]
    before = lax.ppermute(shard[-1:], "row", up)
    after = lax.ppermute(shard[:1], "row", down)
    return jnp.concatenate([before, shard, after], axis=0)


def frame_shift(piece, forward):
    peers = lax.axis_size("frame")
    if forward:
        pairs = [(i, i + 1) for i in range(peers - 1)]
    else:
        pairs = [(i + 1, i) for i in range(peers - 1)]
    return lax.ppermute(piece, "frame", pairs)


def a2a_sum(blocks, axis):
    got = lax.all_to_all(blocks, axis, split_axis=0, concat_axis=0, tiled=True)
    return jnp.sum(got, axis=0)


def staged_scatter(terms):
    n_dp, n_frame, n_row = (lax.axis_size(a) for a in ("dp", "frame", "row"))
    rows = terms.shape[0] // (n_dp * n_frame * n_row)
    chans = terms.shape[-1]
    blocks = terms.reshape(n_dp * n_frame, n_row, rows, chans)
    blocks = jnp.transpose(blocks, (1, 0, 2, 3))
    blocks = a2a_sum(blocks, "row")
    return a2a_sum(blocks, ("dp", "frame"))


def width_taps(a, reverse):
    zero = jnp.zeros_like(a[:, :, :1])
    left = jnp.concatenate([zero, a[:, :, :-1]], axis=2)
    right = jnp.concatenate([a[:, :, 1:], zero], axis=2)
    parts = [right, a, left] if reverse else [left, a, right]
    return jnp.concatenate(parts, axis=-1)


def frame_taps(ext, frames, later):
    if later:
        parts = [ext[:, k : k + frames] for k in range(3)]
    else:
        parts = [ext[:, 2 - k : 2 - k + frames] for k in range(3)]
    return jnp.concatenate(parts, axis=-1)


def on_device(clip_input, cotangent, spatial_weight, temporal_weight):
    x = jnp.transpose(clip_input[0], (1, 0, 2, 3))
    g = jnp.transpose(cotangent[0], (1, 0, 2, 3))
    rows, frames, cols, chans = x.shape
    cells = (
        lax.axis_size("dp") * frames * lax.axis_size("frame") * rows * lax.axis_size("row") * cols
    )
    scale = 1.0 / math.sqrt(cells)
    f32 = jnp.float32
    bf16 = jnp.bfloat16

    x_ext = row_halo(x)
    g_next = frame_shift(g[:, :2], forward=False)
    x3 = width_taps(x_ext, reverse=False)
    fwd_weight = spatial_weight.reshape(3, 3 * chans, chans)
    pre = jnp.zeros((rows * frames * cols, chans), f32)
    for i in range(3):
        piece = x3[i : i + rows].reshape(-1, 3 * chans)
        pre = pre + jnp.dot(piece, fwd_weight[i], preferred_element_type=f32)
    pre = pre.reshape(x.shape)
    act = jax.nn.silu(pre).astype(bf16)
    act_prev = frame_shift(act[:, frames - 2 :], forward=True)
    act3 = frame_taps(jnp.concatenate([act_prev, act], axis=1), frames, later=False)
    g3 = frame_taps(jnp.concatenate([g, g_next], axis=1), frames, later=True)
    act3_flat = act3.reshape(-1, 3 * chans)
    g_flat = g.reshape(-1, chans)

    mixed = jnp.dot(act3_flat, temporal_weight.reshape(3 * chans, chans), preferred_element_type=f32)
    back_temporal = jnp.transpose(temporal_weight, (0, 2, 1)).reshape(3 * chans, chans)
    act_grad = jnp.dot(g3.reshape(-1, 3 * chans), back_temporal, preferred_element_type=f32)
    temporal_grad = lax.dot_general(
        act3_flat, g_flat, (((0,), (0,)), ((), ())), preferred_element_type=f32
    )
    mixed = mixed.astype(bf16).reshape(x.shape)
    act_grad = act_grad.astype(bf16).reshape(x.shape)
    block_output = (x.astype(f32) + mixed.astype(f32)).astype(bf16)

    sigma = jax.nn.sigmoid(pre)
    pre_grad = (act_grad.astype(f32) * sigma * (1.0 + pre * (1.0 - sigma))).astype(bf16)
    pg_flat = pre_grad.reshape(-1, chans)

    spatial_list = []
    for i in range(3):
        piece = x3[i : i + rows].reshape(-1, 3 * chans)
        spatial_list.append(
            lax.dot_general(piece, pg_flat, (((0,), (0,)), ((), ())), preferred_element_type=f32)
        )
    pg3 = width_taps(row_halo(pre_grad), reverse=True)
    back_weight = jnp.transpose(spatial_weight, (0, 1, 3, 2)).reshape(3, 3 * chans, chans)
    back = g.astype(f32).reshape(-1, chans)
    for i in range(3):
        piece = pg3[2 - i : 2 - i + rows].reshape(-1, 3 * chans)
        back = back + jnp.dot(piece, back_weight[i], preferred_element_type=f32)
    input_grad = back.astype(bf16).reshape(x.shape)

    partial_terms = jnp.concatenate(spatial_list + [temporal_grad], axis=0)
    summed = staged_scatter(partial_terms)
    block_output = jnp.transpose(block_output, (1, 0, 2, 3))
    input_grad = jnp.transpose(input_grad, (1, 0, 2, 3))
    return (block_output[None], input_grad[None], summed * scale)


def solution(mesh):
    placed = (P("dp", "frame", "row", None, None), P("dp", "frame", "row", None, None), P(), P())
    return jax.shard_map(
        on_device,
        mesh=mesh,
        in_specs=placed,
        out_specs=(
            P("dp", "frame", "row", None, None),
            P("dp", "frame", "row", None, None),
            P(("dp", "frame", "row"), None),
        ),
        check_vma=False,
    )
```

```python
import math

import jax
import jax.numpy as jnp
from jax import lax
from jax.sharding import PartitionSpec as P


def row_halo(shard):
    peers = lax.axis_size("row")
    up = [(i, i + 1) for i in range(peers - 1)]
    down = [(i + 1, i) for i in range(peers - 1)]
    before = lax.ppermute(shard[-1:], "row", up)
    after = lax.ppermute(shard[:1], "row", down)
    return jnp.concatenate([before, shard, after], axis=0)


def frame_shift(piece, forward):
    peers = lax.axis_size("frame")
    if forward:
        pairs = [(i, i + 1) for i in range(peers - 1)]
    else:
        pairs = [(i + 1, i) for i in range(peers - 1)]
    return lax.ppermute(piece, "frame", pairs)


def a2a_sum(blocks, axis):
    got = lax.all_to_all(blocks, axis, split_axis=0, concat_axis=0, tiled=True)
    return jnp.sum(got, axis=0)


def halving_sum(blocks, axis):
    n = blocks.shape[0]
    me = lax.axis_index(axis)
    bit = 1
    while bit < n:
        mine = (me // bit) % 2
        halves = blocks.reshape((-1, 2) + blocks.shape[1:])
        keep = lax.dynamic_index_in_dim(halves, mine, axis=1, keepdims=False)
        send = lax.dynamic_index_in_dim(halves, 1 - mine, axis=1, keepdims=False)
        got = lax.ppermute(send, axis, [(i, i ^ bit) for i in range(n)])
        blocks = keep + got
        bit *= 2
    return blocks[0]


def staged_scatter(terms):
    n_dp, n_frame, n_row = (lax.axis_size(a) for a in ("dp", "frame", "row"))
    rows = terms.shape[0] // (n_dp * n_frame * n_row)
    chans = terms.shape[-1]
    blocks = terms.reshape(n_dp * n_frame, n_row, rows, chans)
    blocks = jnp.transpose(blocks, (1, 0, 2, 3))
    blocks = halving_sum(blocks, "row")
    return a2a_sum(blocks, ("dp", "frame"))


def width_taps(a, reverse):
    zero = jnp.zeros_like(a[:, :, :1])
    left = jnp.concatenate([zero, a[:, :, :-1]], axis=2)
    right = jnp.concatenate([a[:, :, 1:], zero], axis=2)
    parts = [right, a, left] if reverse else [left, a, right]
    return jnp.concatenate(parts, axis=-1)


def frame_taps(ext, frames, later):
    if later:
        parts = [ext[:, k : k + frames] for k in range(3)]
    else:
        parts = [ext[:, 2 - k : 2 - k + frames] for k in range(3)]
    return jnp.concatenate(parts, axis=-1)


def on_device(clip_input, cotangent, spatial_weight, temporal_weight):
    x = jnp.transpose(clip_input[0], (1, 0, 2, 3))
    g = jnp.transpose(cotangent[0], (1, 0, 2, 3))
    rows, frames, cols, chans = x.shape
    cells = (
        lax.axis_size("dp") * frames * lax.axis_size("frame") * rows * lax.axis_size("row") * cols
    )
    scale = 1.0 / math.sqrt(cells)
    f32 = jnp.float32
    bf16 = jnp.bfloat16

    x_ext = row_halo(x)
    g_next = frame_shift(g[:, :2], forward=False)
    x3 = width_taps(x_ext, reverse=False)
    fwd_weight = spatial_weight.reshape(3, 3 * chans, chans)
    pre = jnp.zeros((rows * frames * cols, chans), f32)
    for i in range(3):
        piece = x3[i : i + rows].reshape(-1, 3 * chans)
        pre = pre + jnp.dot(piece, fwd_weight[i], preferred_element_type=f32)
    pre = pre.reshape(x.shape)
    act = jax.nn.silu(pre).astype(bf16)
    act_prev = frame_shift(act[:, frames - 2 :], forward=True)
    act3 = frame_taps(jnp.concatenate([act_prev, act], axis=1), frames, later=False)
    g3 = frame_taps(jnp.concatenate([g, g_next], axis=1), frames, later=True)
    act3_flat = act3.reshape(-1, 3 * chans)
    g_flat = g.reshape(-1, chans)

    mixed = jnp.dot(act3_flat, temporal_weight.reshape(3 * chans, chans), preferred_element_type=f32)
    back_temporal = jnp.transpose(temporal_weight, (0, 2, 1)).reshape(3 * chans, chans)
    act_grad = jnp.dot(g3.reshape(-1, 3 * chans), back_temporal, preferred_element_type=f32)
    temporal_grad = lax.dot_general(
        act3_flat, g_flat, (((0,), (0,)), ((), ())), preferred_element_type=f32
    )
    mixed = mixed.astype(bf16).reshape(x.shape)
    act_grad = act_grad.astype(bf16).reshape(x.shape)
    block_output = (x.astype(f32) + mixed.astype(f32)).astype(bf16)

    sigma = jax.nn.sigmoid(pre)
    pre_grad = (act_grad.astype(f32) * sigma * (1.0 + pre * (1.0 - sigma))).astype(bf16)
    pg_flat = pre_grad.reshape(-1, chans)

    spatial_list = []
    for i in range(3):
        piece = x3[i : i + rows].reshape(-1, 3 * chans)
        spatial_list.append(
            lax.dot_general(piece, pg_flat, (((0,), (0,)), ((), ())), preferred_element_type=f32)
        )
    pg3 = width_taps(row_halo(pre_grad), reverse=True)
    back_weight = jnp.transpose(spatial_weight, (0, 1, 3, 2)).reshape(3, 3 * chans, chans)
    back = g.astype(f32).reshape(-1, chans)
    for i in range(3):
        piece = pg3[2 - i : 2 - i + rows].reshape(-1, 3 * chans)
        back = back + jnp.dot(piece, back_weight[i], preferred_element_type=f32)
    input_grad = back.astype(bf16).reshape(x.shape)

    partial_terms = jnp.concatenate(spatial_list + [temporal_grad], axis=0)
    summed = staged_scatter(partial_terms)
    block_output = jnp.transpose(block_output, (1, 0, 2, 3))
    input_grad = jnp.transpose(input_grad, (1, 0, 2, 3))
    return (block_output[None], input_grad[None], summed * scale)


def solution(mesh):
    placed = (P("dp", "frame", "row", None, None), P("dp", "frame", "row", None, None), P(), P())
    return jax.shard_map(
        on_device,
        mesh=mesh,
        in_specs=placed,
        out_specs=(
            P("dp", "frame", "row", None, None),
            P("dp", "frame", "row", None, None),
            P(("dp", "frame", "row"), None),
        ),
        check_vma=False,
    )
```

```python
import math

import jax
import jax.numpy as jnp
from jax import lax
from jax.sharding import PartitionSpec as P


def frame_shift(piece, forward):
    peers = lax.axis_size("frame")
    if forward:
        pairs = [(i, i + 1) for i in range(peers - 1)]
    else:
        pairs = [(i + 1, i) for i in range(peers - 1)]
    return lax.ppermute(piece, "frame", pairs)


def a2a_sum(blocks, axis):
    got = lax.all_to_all(blocks, axis, split_axis=0, concat_axis=0, tiled=True)
    return jnp.sum(got, axis=0)


def halving_sum(blocks, axis):
    n = blocks.shape[0]
    me = lax.axis_index(axis)
    bit = 1
    while bit < n:
        mine = (me // bit) % 2
        halves = blocks.reshape((-1, 2) + blocks.shape[1:])
        keep = lax.dynamic_index_in_dim(halves, mine, axis=1, keepdims=False)
        send = lax.dynamic_index_in_dim(halves, 1 - mine, axis=1, keepdims=False)
        got = lax.ppermute(send, axis, [(i, i ^ bit) for i in range(n)])
        blocks = keep + got
        bit *= 2
    return blocks[0]


def staged_scatter(terms):
    n_dp, n_frame, n_row = (lax.axis_size(a) for a in ("dp", "frame", "row"))
    rows = terms.shape[0] // (n_dp * n_frame * n_row)
    chans = terms.shape[-1]
    blocks = terms.reshape(n_dp * n_frame, n_row, rows, chans)
    blocks = jnp.transpose(blocks, (1, 0, 2, 3))
    blocks = halving_sum(blocks, "row")
    return a2a_sum(blocks, ("dp", "frame"))


def width_taps(a, reverse):
    zero = jnp.zeros_like(a[:, :, :1])
    left = jnp.concatenate([zero, a[:, :, :-1]], axis=2)
    right = jnp.concatenate([a[:, :, 1:], zero], axis=2)
    parts = [right, a, left] if reverse else [left, a, right]
    return jnp.concatenate(parts, axis=-1)


def frame_taps(ext, frames, later):
    if later:
        parts = [ext[:, k : k + frames] for k in range(3)]
    else:
        parts = [ext[:, 2 - k : 2 - k + frames] for k in range(3)]
    return jnp.concatenate(parts, axis=-1)


def on_device(clip_input, cotangent, spatial_weight, temporal_weight):
    x = jnp.transpose(clip_input[0], (1, 0, 2, 3))
    g = jnp.transpose(cotangent[0], (1, 0, 2, 3))
    rows, frames, cols, chans = x.shape
    cells = (
        lax.axis_size("dp") * frames * lax.axis_size("frame") * rows * lax.axis_size("row") * cols
    )
    scale = 1.0 / math.sqrt(cells)
    f32 = jnp.float32
    bf16 = jnp.bfloat16

    peers = lax.axis_size("row")
    above = lax.ppermute(
        jnp.concatenate([x[rows - 2 :], g[rows - 1 :]], axis=0), "row",
        [(i, i + 1) for i in range(peers - 1)],
    )
    below = lax.ppermute(
        jnp.concatenate([x[:2], g[:1]], axis=0), "row", [(i + 1, i) for i in range(peers - 1)]
    )
    x_e = jnp.concatenate([above[:2], x, below[:2]], axis=0)
    g_e = jnp.concatenate([above[2:], g, below[2:]], axis=0)
    g_next = frame_shift(g_e[:, :2], forward=False)

    x3 = width_taps(x_e, reverse=False)
    fwd_weight = spatial_weight.reshape(3, 3 * chans, chans)
    wide = (rows + 2, frames, cols, chans)
    pre = jnp.zeros((math.prod(wide[:-1]), chans), f32)
    for i in range(3):
        piece = x3[i : i + rows + 2].reshape(-1, 3 * chans)
        pre = pre + jnp.dot(piece, fwd_weight[i], preferred_element_type=f32)
    pre = pre.reshape(wide)
    act = jax.nn.silu(pre[1 : rows + 1]).astype(bf16)
    act_prev = frame_shift(act[:, frames - 2 :], forward=True)
    act3 = frame_taps(jnp.concatenate([act_prev, act], axis=1), frames, later=False)
    g3 = frame_taps(jnp.concatenate([g_e, g_next], axis=1), frames, later=True)
    act3_flat = act3.reshape(-1, 3 * chans)
    g_flat = g.reshape(-1, chans)

    mixed = jnp.dot(act3_flat, temporal_weight.reshape(3 * chans, chans), preferred_element_type=f32)
    back_temporal = jnp.transpose(temporal_weight, (0, 2, 1)).reshape(3 * chans, chans)
    act_grad = jnp.dot(g3.reshape(-1, 3 * chans), back_temporal, preferred_element_type=f32)
    temporal_grad = lax.dot_general(
        act3_flat, g_flat, (((0,), (0,)), ((), ())), preferred_element_type=f32
    )
    mixed = mixed.astype(bf16).reshape(x.shape)
    act_grad = act_grad.astype(bf16).reshape(wide)
    block_output = (x.astype(f32) + mixed.astype(f32)).astype(bf16)

    sigma = jax.nn.sigmoid(pre)
    pg_ext = (act_grad.astype(f32) * sigma * (1.0 + pre * (1.0 - sigma))).astype(bf16)
    pg_flat = pg_ext[1 : rows + 1].reshape(-1, chans)

    spatial_list = []
    for i in range(3):
        piece = x3[1 + i : 1 + i + rows].reshape(-1, 3 * chans)
        spatial_list.append(
            lax.dot_general(piece, pg_flat, (((0,), (0,)), ((), ())), preferred_element_type=f32)
        )
    pg3 = width_taps(pg_ext, reverse=True)
    back_weight = jnp.transpose(spatial_weight, (0, 1, 3, 2)).reshape(3, 3 * chans, chans)
    back = g.astype(f32).reshape(-1, chans)
    for i in range(3):
        piece = pg3[2 - i : 2 - i + rows].reshape(-1, 3 * chans)
        back = back + jnp.dot(piece, back_weight[i], preferred_element_type=f32)
    input_grad = back.astype(bf16).reshape(x.shape)

    partial_terms = jnp.concatenate(spatial_list + [temporal_grad], axis=0)
    summed = staged_scatter(partial_terms)
    block_output = jnp.transpose(block_output, (1, 0, 2, 3))
    input_grad = jnp.transpose(input_grad, (1, 0, 2, 3))
    return (block_output[None], input_grad[None], summed * scale)


def solution(mesh):
    placed = (P("dp", "frame", "row", None, None), P("dp", "frame", "row", None, None), P(), P())
    return jax.shard_map(
        on_device,
        mesh=mesh,
        in_specs=placed,
        out_specs=(
            P("dp", "frame", "row", None, None),
            P("dp", "frame", "row", None, None),
            P(("dp", "frame", "row"), None),
        ),
        check_vma=False,
    )
```

```python
import math

import jax
import jax.numpy as jnp
from jax import lax
from jax.sharding import PartitionSpec as P


def frame_shift(piece, forward):
    peers = lax.axis_size("frame")
    if forward:
        pairs = [(i, i + 1) for i in range(peers - 1)]
    else:
        pairs = [(i + 1, i) for i in range(peers - 1)]
    return lax.ppermute(piece, "frame", pairs)


def grid_shift(piece, df, dr):
    n_f, n_r = lax.axis_size("frame"), lax.axis_size("row")
    pairs = [
        (f * n_r + r, (f + df) * n_r + (r + dr))
        for f in range(n_f)
        for r in range(n_r)
        if 0 <= f + df < n_f and 0 <= r + dr < n_r
    ]
    return lax.ppermute(piece, ("frame", "row"), pairs)


def a2a_sum(blocks, axis):
    got = lax.all_to_all(blocks, axis, split_axis=0, concat_axis=0, tiled=True)
    return jnp.sum(got, axis=0)


def halving_sum(blocks, axis):
    n = blocks.shape[0]
    me = lax.axis_index(axis)
    bit = 1
    while bit < n:
        mine = (me // bit) % 2
        halves = blocks.reshape((-1, 2) + blocks.shape[1:])
        keep = lax.dynamic_index_in_dim(halves, mine, axis=1, keepdims=False)
        send = lax.dynamic_index_in_dim(halves, 1 - mine, axis=1, keepdims=False)
        got = lax.ppermute(send, axis, [(i, i ^ bit) for i in range(n)])
        blocks = keep + got
        bit *= 2
    return blocks[0]


def staged_scatter(terms):
    n_dp, n_frame, n_row = (lax.axis_size(a) for a in ("dp", "frame", "row"))
    rows = terms.shape[0] // (n_dp * n_frame * n_row)
    chans = terms.shape[-1]
    blocks = terms.reshape(n_dp * n_frame, n_row, rows, chans)
    blocks = jnp.transpose(blocks, (1, 0, 2, 3))
    blocks = halving_sum(blocks, "row")
    return a2a_sum(blocks, ("dp", "frame"))


def width_taps(a, reverse):
    zero = jnp.zeros_like(a[:, :, :1])
    left = jnp.concatenate([zero, a[:, :, :-1]], axis=2)
    right = jnp.concatenate([a[:, :, 1:], zero], axis=2)
    parts = [right, a, left] if reverse else [left, a, right]
    return jnp.concatenate(parts, axis=-1)


def frame_taps(ext, frames, later):
    if later:
        parts = [ext[:, k : k + frames] for k in range(3)]
    else:
        parts = [ext[:, 2 - k : 2 - k + frames] for k in range(3)]
    return jnp.concatenate(parts, axis=-1)


def on_device(clip_input, cotangent, spatial_weight, temporal_weight):
    x = jnp.transpose(clip_input[0], (1, 0, 2, 3))
    g = jnp.transpose(cotangent[0], (1, 0, 2, 3))
    rows, frames, cols, chans = x.shape
    cells = (
        lax.axis_size("dp") * frames * lax.axis_size("frame") * rows * lax.axis_size("row") * cols
    )
    scale = 1.0 / math.sqrt(cells)
    f32 = jnp.float32
    bf16 = jnp.bfloat16

    peers = lax.axis_size("row")
    above = lax.ppermute(
        jnp.concatenate([x[rows - 2 :], g[rows - 1 :]], axis=0), "row",
        [(i, i + 1) for i in range(peers - 1)],
    )
    below = lax.ppermute(
        jnp.concatenate([x[:2], g[:1]], axis=0), "row", [(i + 1, i) for i in range(peers - 1)]
    )
    g_next = jnp.concatenate(
        [
            grid_shift(g[rows - 1 :, :2], -1, 1),
            grid_shift(g[:, :2], -1, 0),
            grid_shift(g[:1, :2], -1, -1),
        ],
        axis=0,
    )
    x_e = jnp.concatenate([above[:2], x, below[:2]], axis=0)
    g_e = jnp.concatenate([above[2:], g, below[2:]], axis=0)

    x3 = width_taps(x_e, reverse=False)
    fwd_weight = spatial_weight.reshape(3, 3 * chans, chans)
    wide = (rows + 2, frames, cols, chans)
    pre = jnp.zeros((math.prod(wide[:-1]), chans), f32)
    for i in range(3):
        piece = x3[i : i + rows + 2].reshape(-1, 3 * chans)
        pre = pre + jnp.dot(piece, fwd_weight[i], preferred_element_type=f32)
    pre = pre.reshape(wide)
    act = jax.nn.silu(pre[1 : rows + 1]).astype(bf16)
    act_prev = frame_shift(act[:, frames - 2 :], forward=True)
    act3 = frame_taps(jnp.concatenate([act_prev, act], axis=1), frames, later=False)
    g3 = frame_taps(jnp.concatenate([g_e, g_next], axis=1), frames, later=True)
    act3_flat = act3.reshape(-1, 3 * chans)
    g_flat = g.reshape(-1, chans)

    mixed = jnp.dot(act3_flat, temporal_weight.reshape(3 * chans, chans), preferred_element_type=f32)
    back_temporal = jnp.transpose(temporal_weight, (0, 2, 1)).reshape(3 * chans, chans)
    act_grad = jnp.dot(g3.reshape(-1, 3 * chans), back_temporal, preferred_element_type=f32)
    temporal_grad = lax.dot_general(
        act3_flat, g_flat, (((0,), (0,)), ((), ())), preferred_element_type=f32
    )
    mixed = mixed.astype(bf16).reshape(x.shape)
    act_grad = act_grad.astype(bf16).reshape(wide)
    block_output = (x.astype(f32) + mixed.astype(f32)).astype(bf16)

    sigma = jax.nn.sigmoid(pre)
    pg_ext = (act_grad.astype(f32) * sigma * (1.0 + pre * (1.0 - sigma))).astype(bf16)
    pg_flat = pg_ext[1 : rows + 1].reshape(-1, chans)

    spatial_list = []
    for i in range(3):
        piece = x3[1 + i : 1 + i + rows].reshape(-1, 3 * chans)
        spatial_list.append(
            lax.dot_general(piece, pg_flat, (((0,), (0,)), ((), ())), preferred_element_type=f32)
        )
    pg3 = width_taps(pg_ext, reverse=True)
    back_weight = jnp.transpose(spatial_weight, (0, 1, 3, 2)).reshape(3, 3 * chans, chans)
    back = g.astype(f32).reshape(-1, chans)
    for i in range(3):
        piece = pg3[2 - i : 2 - i + rows].reshape(-1, 3 * chans)
        back = back + jnp.dot(piece, back_weight[i], preferred_element_type=f32)
    input_grad = back.astype(bf16).reshape(x.shape)

    partial_terms = jnp.concatenate(spatial_list + [temporal_grad], axis=0)
    summed = staged_scatter(partial_terms)
    block_output = jnp.transpose(block_output, (1, 0, 2, 3))
    input_grad = jnp.transpose(input_grad, (1, 0, 2, 3))
    return (block_output[None], input_grad[None], summed * scale)


def solution(mesh):
    placed = (P("dp", "frame", "row", None, None), P("dp", "frame", "row", None, None), P(), P())
    return jax.shard_map(
        on_device,
        mesh=mesh,
        in_specs=placed,
        out_specs=(
            P("dp", "frame", "row", None, None),
            P("dp", "frame", "row", None, None),
            P(("dp", "frame", "row"), None),
        ),
        check_vma=False,
    )
```

```python
import math

import jax
import jax.numpy as jnp
from jax import lax
from jax.sharding import PartitionSpec as P


def row_halo(shard):
    peers = lax.axis_size("row")
    up = [(i, i + 1) for i in range(peers - 1)]
    down = [(i + 1, i) for i in range(peers - 1)]
    before = lax.ppermute(shard[-1:], "row", up)
    after = lax.ppermute(shard[:1], "row", down)
    return jnp.concatenate([before, shard, after], axis=0)


def frame_shift(piece, forward):
    peers = lax.axis_size("frame")
    if forward:
        pairs = [(i, i + 1) for i in range(peers - 1)]
    else:
        pairs = [(i + 1, i) for i in range(peers - 1)]
    return lax.ppermute(piece, "frame", pairs)


def a2a_sum(blocks, axis):
    got = lax.all_to_all(blocks, axis, split_axis=0, concat_axis=0, tiled=True)
    return jnp.sum(got, axis=0)


def halving_sum(blocks, axis):
    n = blocks.shape[0]
    me = lax.axis_index(axis)
    bit = 1
    while bit < n:
        mine = (me // bit) % 2
        halves = blocks.reshape((-1, 2) + blocks.shape[1:])
        keep = lax.dynamic_index_in_dim(halves, mine, axis=1, keepdims=False)
        send = lax.dynamic_index_in_dim(halves, 1 - mine, axis=1, keepdims=False)
        got = lax.ppermute(send, axis, [(i, i ^ bit) for i in range(n)])
        blocks = keep + got
        bit *= 2
    return blocks[0]


def staged_scatter(terms):
    n_dp, n_frame, n_row = (lax.axis_size(a) for a in ("dp", "frame", "row"))
    rows = terms.shape[0] // (n_dp * n_frame * n_row)
    chans = terms.shape[-1]
    blocks = terms.reshape(n_dp * n_frame, n_row * rows, chans)
    blocks = a2a_sum(blocks, ("dp", "frame"))
    return halving_sum(blocks.reshape(n_row, rows, chans), "row")


def width_taps(a, reverse):
    zero = jnp.zeros_like(a[:, :, :1])
    left = jnp.concatenate([zero, a[:, :, :-1]], axis=2)
    right = jnp.concatenate([a[:, :, 1:], zero], axis=2)
    parts = [right, a, left] if reverse else [left, a, right]
    return jnp.concatenate(parts, axis=-1)


def frame_taps(ext, frames, later):
    if later:
        parts = [ext[:, k : k + frames] for k in range(3)]
    else:
        parts = [ext[:, 2 - k : 2 - k + frames] for k in range(3)]
    return jnp.concatenate(parts, axis=-1)


def on_device(clip_input, cotangent, spatial_weight, temporal_weight):
    x = jnp.transpose(clip_input[0], (1, 0, 2, 3))
    g = jnp.transpose(cotangent[0], (1, 0, 2, 3))
    rows, frames, cols, chans = x.shape
    cells = (
        lax.axis_size("dp") * frames * lax.axis_size("frame") * rows * lax.axis_size("row") * cols
    )
    scale = 1.0 / math.sqrt(cells)
    f32 = jnp.float32
    bf16 = jnp.bfloat16

    x_ext = row_halo(x)
    g_next = frame_shift(g[:, :2], forward=False)
    x3 = width_taps(x_ext, reverse=False)
    fwd_weight = spatial_weight.reshape(3, 3 * chans, chans)
    pre = jnp.zeros((rows * frames * cols, chans), f32)
    for i in range(3):
        piece = x3[i : i + rows].reshape(-1, 3 * chans)
        pre = pre + jnp.dot(piece, fwd_weight[i], preferred_element_type=f32)
    pre = pre.reshape(x.shape)
    act = jax.nn.silu(pre).astype(bf16)
    act_prev = frame_shift(act[:, frames - 2 :], forward=True)
    act3 = frame_taps(jnp.concatenate([act_prev, act], axis=1), frames, later=False)
    g3 = frame_taps(jnp.concatenate([g, g_next], axis=1), frames, later=True)
    act3_flat = act3.reshape(-1, 3 * chans)
    g_flat = g.reshape(-1, chans)

    mixed = jnp.dot(act3_flat, temporal_weight.reshape(3 * chans, chans), preferred_element_type=f32)
    back_temporal = jnp.transpose(temporal_weight, (0, 2, 1)).reshape(3 * chans, chans)
    act_grad = jnp.dot(g3.reshape(-1, 3 * chans), back_temporal, preferred_element_type=f32)
    temporal_grad = lax.dot_general(
        act3_flat, g_flat, (((0,), (0,)), ((), ())), preferred_element_type=f32
    )
    mixed = mixed.astype(bf16).reshape(x.shape)
    act_grad = act_grad.astype(bf16).reshape(x.shape)
    block_output = (x.astype(f32) + mixed.astype(f32)).astype(bf16)

    sigma = jax.nn.sigmoid(pre)
    pre_grad = (act_grad.astype(f32) * sigma * (1.0 + pre * (1.0 - sigma))).astype(bf16)
    pg_flat = pre_grad.reshape(-1, chans)

    spatial_list = []
    for i in range(3):
        piece = x3[i : i + rows].reshape(-1, 3 * chans)
        spatial_list.append(
            lax.dot_general(piece, pg_flat, (((0,), (0,)), ((), ())), preferred_element_type=f32)
        )
    pg3 = width_taps(row_halo(pre_grad), reverse=True)
    back_weight = jnp.transpose(spatial_weight, (0, 1, 3, 2)).reshape(3, 3 * chans, chans)
    back = g.astype(f32).reshape(-1, chans)
    for i in range(3):
        piece = pg3[2 - i : 2 - i + rows].reshape(-1, 3 * chans)
        back = back + jnp.dot(piece, back_weight[i], preferred_element_type=f32)
    input_grad = back.astype(bf16).reshape(x.shape)

    partial_terms = jnp.concatenate(spatial_list + [temporal_grad], axis=0)
    summed = staged_scatter(partial_terms)
    block_output = jnp.transpose(block_output, (1, 0, 2, 3))
    input_grad = jnp.transpose(input_grad, (1, 0, 2, 3))
    return (block_output[None], input_grad[None], summed * scale)


def solution(mesh):
    placed = (P("dp", "frame", "row", None, None), P("dp", "frame", "row", None, None), P(), P())
    return jax.shard_map(
        on_device,
        mesh=mesh,
        in_specs=placed,
        out_specs=(
            P("dp", "frame", "row", None, None),
            P("dp", "frame", "row", None, None),
            P(("dp", "frame", "row"), None),
        ),
        check_vma=False,
    )
```

```python
import math

import jax
import jax.numpy as jnp
from jax import lax
from jax.sharding import PartitionSpec as P


def row_halo(shard):
    peers = lax.axis_size("row")
    up = [(i, i + 1) for i in range(peers - 1)]
    down = [(i + 1, i) for i in range(peers - 1)]
    before = lax.ppermute(shard[-1:], "row", up)
    after = lax.ppermute(shard[:1], "row", down)
    return jnp.concatenate([before, shard, after], axis=0)


def frame_shift(piece, forward):
    peers = lax.axis_size("frame")
    if forward:
        pairs = [(i, i + 1) for i in range(peers - 1)]
    else:
        pairs = [(i + 1, i) for i in range(peers - 1)]
    return lax.ppermute(piece, "frame", pairs)


def a2a_sum(blocks, axis):
    got = lax.all_to_all(blocks, axis, split_axis=0, concat_axis=0, tiled=True)
    return jnp.sum(got, axis=0)


def halving_sum(blocks, axis):
    n = blocks.shape[0]
    me = lax.axis_index(axis)
    bit = 1
    while bit < n:
        mine = (me // bit) % 2
        halves = blocks.reshape((-1, 2) + blocks.shape[1:])
        keep = lax.dynamic_index_in_dim(halves, mine, axis=1, keepdims=False)
        send = lax.dynamic_index_in_dim(halves, 1 - mine, axis=1, keepdims=False)
        got = lax.ppermute(send, axis, [(i, i ^ bit) for i in range(n)])
        blocks = keep + got
        bit *= 2
    return blocks[0]


def staged_scatter(terms):
    n_dp, n_frame, n_row = (lax.axis_size(a) for a in ("dp", "frame", "row"))
    rows = terms.shape[0] // (n_dp * n_frame * n_row)
    chans = terms.shape[-1]
    blocks = terms.reshape(n_dp * n_frame, n_row * rows, chans)
    blocks = a2a_sum(blocks, ("dp", "frame"))
    return a2a_sum(blocks.reshape(n_row, rows, chans), "row")


def width_taps(a, reverse):
    zero = jnp.zeros_like(a[:, :, :1])
    left = jnp.concatenate([zero, a[:, :, :-1]], axis=2)
    right = jnp.concatenate([a[:, :, 1:], zero], axis=2)
    parts = [right, a, left] if reverse else [left, a, right]
    return jnp.concatenate(parts, axis=-1)


def frame_taps(ext, frames, later):
    if later:
        parts = [ext[:, k : k + frames] for k in range(3)]
    else:
        parts = [ext[:, 2 - k : 2 - k + frames] for k in range(3)]
    return jnp.concatenate(parts, axis=-1)


def on_device(clip_input, cotangent, spatial_weight, temporal_weight):
    x = jnp.transpose(clip_input[0], (1, 0, 2, 3))
    g = jnp.transpose(cotangent[0], (1, 0, 2, 3))
    rows, frames, cols, chans = x.shape
    cells = (
        lax.axis_size("dp") * frames * lax.axis_size("frame") * rows * lax.axis_size("row") * cols
    )
    scale = 1.0 / math.sqrt(cells)
    f32 = jnp.float32
    bf16 = jnp.bfloat16

    x_ext = row_halo(x)
    g_next = frame_shift(g[:, :2], forward=False)
    x3 = width_taps(x_ext, reverse=False)
    fwd_weight = spatial_weight.reshape(3, 3 * chans, chans)
    pre = jnp.zeros((rows * frames * cols, chans), f32)
    for i in range(3):
        piece = x3[i : i + rows].reshape(-1, 3 * chans)
        pre = pre + jnp.dot(piece, fwd_weight[i], preferred_element_type=f32)
    pre = pre.reshape(x.shape)
    act = jax.nn.silu(pre).astype(bf16)
    act_prev = frame_shift(act[:, frames - 2 :], forward=True)
    act3 = frame_taps(jnp.concatenate([act_prev, act], axis=1), frames, later=False)
    g3 = frame_taps(jnp.concatenate([g, g_next], axis=1), frames, later=True)
    act3_flat = act3.reshape(-1, 3 * chans)
    g_flat = g.reshape(-1, chans)

    mixed = jnp.dot(act3_flat, temporal_weight.reshape(3 * chans, chans), preferred_element_type=f32)
    back_temporal = jnp.transpose(temporal_weight, (0, 2, 1)).reshape(3 * chans, chans)
    act_grad = jnp.dot(g3.reshape(-1, 3 * chans), back_temporal, preferred_element_type=f32)
    temporal_grad = lax.dot_general(
        act3_flat, g_flat, (((0,), (0,)), ((), ())), preferred_element_type=f32
    )
    mixed = mixed.astype(bf16).reshape(x.shape)
    act_grad = act_grad.astype(bf16).reshape(x.shape)
    block_output = (x.astype(f32) + mixed.astype(f32)).astype(bf16)

    sigma = jax.nn.sigmoid(pre)
    pre_grad = (act_grad.astype(f32) * sigma * (1.0 + pre * (1.0 - sigma))).astype(bf16)
    pg_flat = pre_grad.reshape(-1, chans)

    spatial_list = []
    for i in range(3):
        piece = x3[i : i + rows].reshape(-1, 3 * chans)
        spatial_list.append(
            lax.dot_general(piece, pg_flat, (((0,), (0,)), ((), ())), preferred_element_type=f32)
        )
    pg3 = width_taps(row_halo(pre_grad), reverse=True)
    back_weight = jnp.transpose(spatial_weight, (0, 1, 3, 2)).reshape(3, 3 * chans, chans)
    back = g.astype(f32).reshape(-1, chans)
    for i in range(3):
        piece = pg3[2 - i : 2 - i + rows].reshape(-1, 3 * chans)
        back = back + jnp.dot(piece, back_weight[i], preferred_element_type=f32)
    input_grad = back.astype(bf16).reshape(x.shape)

    partial_terms = jnp.concatenate(spatial_list + [temporal_grad], axis=0)
    summed = staged_scatter(partial_terms)
    block_output = jnp.transpose(block_output, (1, 0, 2, 3))
    input_grad = jnp.transpose(input_grad, (1, 0, 2, 3))
    return (block_output[None], input_grad[None], summed * scale)


def solution(mesh):
    placed = (P("dp", "frame", "row", None, None), P("dp", "frame", "row", None, None), P(), P())
    return jax.shard_map(
        on_device,
        mesh=mesh,
        in_specs=placed,
        out_specs=(
            P("dp", "frame", "row", None, None),
            P("dp", "frame", "row", None, None),
            P(("dp", "frame", "row"), None),
        ),
        check_vma=False,
    )
```

```python
import math

import jax
import jax.numpy as jnp
from jax import lax
from jax.sharding import PartitionSpec as P


def row_halo(shard):
    peers = lax.axis_size("row")
    up = [(i, i + 1) for i in range(peers - 1)]
    down = [(i + 1, i) for i in range(peers - 1)]
    before = lax.ppermute(shard[-1:], "row", up)
    after = lax.ppermute(shard[:1], "row", down)
    return jnp.concatenate([before, shard, after], axis=0)


def frame_shift(piece, forward):
    peers = lax.axis_size("frame")
    if forward:
        pairs = [(i, i + 1) for i in range(peers - 1)]
    else:
        pairs = [(i + 1, i) for i in range(peers - 1)]
    return lax.ppermute(piece, "frame", pairs)


def a2a_sum(blocks, axis):
    got = lax.all_to_all(blocks, axis, split_axis=0, concat_axis=0, tiled=True)
    return jnp.sum(got, axis=0)


def halving_sum(blocks, axis):
    n = blocks.shape[0]
    me = lax.axis_index(axis)
    bit = 1
    while bit < n:
        mine = (me // bit) % 2
        halves = blocks.reshape((-1, 2) + blocks.shape[1:])
        keep = lax.dynamic_index_in_dim(halves, mine, axis=1, keepdims=False)
        send = lax.dynamic_index_in_dim(halves, 1 - mine, axis=1, keepdims=False)
        got = lax.ppermute(send, axis, [(i, i ^ bit) for i in range(n)])
        blocks = keep + got
        bit *= 2
    return blocks[0]


def staged_scatter(terms):
    n_dp, n_frame, n_row = (lax.axis_size(a) for a in ("dp", "frame", "row"))
    rows = terms.shape[0] // (n_dp * n_frame * n_row)
    chans = terms.shape[-1]
    blocks = terms.reshape(n_dp * n_frame, n_row * rows, chans)
    blocks = a2a_sum(blocks, ("dp", "frame"))
    return halving_sum(blocks.reshape(n_row, rows, chans), "row")


def width_taps(a, reverse):
    zero = jnp.zeros_like(a[:, :, :1])
    left = jnp.concatenate([zero, a[:, :, :-1]], axis=2)
    right = jnp.concatenate([a[:, :, 1:], zero], axis=2)
    parts = [right, a, left] if reverse else [left, a, right]
    return jnp.concatenate(parts, axis=-1)


def frame_taps(ext, frames, later):
    if later:
        parts = [ext[:, k : k + frames] for k in range(3)]
    else:
        parts = [ext[:, 2 - k : 2 - k + frames] for k in range(3)]
    return jnp.concatenate(parts, axis=-1)


def on_device(clip_input, cotangent, spatial_weight, temporal_weight):
    x = jnp.transpose(clip_input[0], (1, 0, 2, 3))
    g = jnp.transpose(cotangent[0], (1, 0, 2, 3))
    rows, frames, cols, chans = x.shape
    cells = (
        lax.axis_size("dp") * frames * lax.axis_size("frame") * rows * lax.axis_size("row") * cols
    )
    scale = 1.0 / math.sqrt(cells)
    f32 = jnp.float32
    bf16 = jnp.bfloat16

    x_ext = row_halo(x)
    g_next = frame_shift(g[:, :2], forward=False)
    x3 = width_taps(x_ext, reverse=False)
    fwd_weight = spatial_weight.reshape(3, 3 * chans, chans)
    x9 = jnp.concatenate([x3[i : i + rows] for i in range(3)], axis=-1).reshape(-1, 9 * chans)
    pre = jnp.dot(x9, fwd_weight.reshape(9 * chans, chans), preferred_element_type=f32)
    pre = pre.reshape(x.shape)
    act = jax.nn.silu(pre).astype(bf16)
    act_prev = frame_shift(act[:, frames - 2 :], forward=True)
    act3 = frame_taps(jnp.concatenate([act_prev, act], axis=1), frames, later=False)
    g3 = frame_taps(jnp.concatenate([g, g_next], axis=1), frames, later=True)
    act3_flat = act3.reshape(-1, 3 * chans)
    g_flat = g.reshape(-1, chans)

    mixed = jnp.dot(act3_flat, temporal_weight.reshape(3 * chans, chans), preferred_element_type=f32)
    back_temporal = jnp.transpose(temporal_weight, (0, 2, 1)).reshape(3 * chans, chans)
    act_grad = jnp.dot(g3.reshape(-1, 3 * chans), back_temporal, preferred_element_type=f32)
    temporal_grad = lax.dot_general(
        act3_flat, g_flat, (((0,), (0,)), ((), ())), preferred_element_type=f32
    )
    mixed = mixed.astype(bf16).reshape(x.shape)
    act_grad = act_grad.astype(bf16).reshape(x.shape)
    block_output = (x.astype(f32) + mixed.astype(f32)).astype(bf16)

    sigma = jax.nn.sigmoid(pre)
    pre_grad = (act_grad.astype(f32) * sigma * (1.0 + pre * (1.0 - sigma))).astype(bf16)
    pg_flat = pre_grad.reshape(-1, chans)

    spatial_grad = lax.dot_general(x9, pg_flat, (((0,), (0,)), ((), ())), preferred_element_type=f32)
    pg3 = width_taps(row_halo(pre_grad), reverse=True)
    back_weight = jnp.transpose(spatial_weight, (0, 1, 3, 2)).reshape(3, 3 * chans, chans)
    pg9 = jnp.concatenate([pg3[2 - i : 2 - i + rows] for i in range(3)], axis=-1).reshape(-1, 9 * chans)
    back = g.astype(f32).reshape(-1, chans) + jnp.dot(
        pg9, back_weight.reshape(9 * chans, chans), preferred_element_type=f32
    )
    input_grad = back.astype(bf16).reshape(x.shape)

    partial_terms = jnp.concatenate([spatial_grad, temporal_grad], axis=0)
    summed = staged_scatter(partial_terms)
    block_output = jnp.transpose(block_output, (1, 0, 2, 3))
    input_grad = jnp.transpose(input_grad, (1, 0, 2, 3))
    return (block_output[None], input_grad[None], summed * scale)


def solution(mesh):
    placed = (P("dp", "frame", "row", None, None), P("dp", "frame", "row", None, None), P(), P())
    return jax.shard_map(
        on_device,
        mesh=mesh,
        in_specs=placed,
        out_specs=(
            P("dp", "frame", "row", None, None),
            P("dp", "frame", "row", None, None),
            P(("dp", "frame", "row"), None),
        ),
        check_vma=False,
    )
```

```python
import math

import jax
import jax.numpy as jnp
from jax import lax
from jax.sharding import PartitionSpec as P


def row_halo(shard):
    peers = lax.axis_size("row")
    up = [(i, i + 1) for i in range(peers - 1)]
    down = [(i + 1, i) for i in range(peers - 1)]
    before = lax.ppermute(shard[-1:], "row", up)
    after = lax.ppermute(shard[:1], "row", down)
    return jnp.concatenate([before, shard, after], axis=0)


def frame_shift(piece, forward):
    peers = lax.axis_size("frame")
    if forward:
        pairs = [(i, i + 1) for i in range(peers - 1)]
    else:
        pairs = [(i + 1, i) for i in range(peers - 1)]
    return lax.ppermute(piece, "frame", pairs)


def a2a_sum(blocks, axis):
    got = lax.all_to_all(blocks, axis, split_axis=0, concat_axis=0, tiled=True)
    return jnp.sum(got, axis=0)


def halving_sum(blocks, axis):
    n = blocks.shape[0]
    me = lax.axis_index(axis)
    bit = n // 2
    while bit >= 1:
        mine = (me // bit) % 2
        halves = blocks.reshape((2, -1) + blocks.shape[1:])
        keep = lax.dynamic_index_in_dim(halves, mine, axis=0, keepdims=False)
        send = lax.dynamic_index_in_dim(halves, 1 - mine, axis=0, keepdims=False)
        got = lax.ppermute(send, axis, [(i, i ^ bit) for i in range(n)])
        blocks = keep + got
        bit //= 2
    return blocks[0]


def staged_scatter(terms):
    n_dp, n_frame, n_row = (lax.axis_size(a) for a in ("dp", "frame", "row"))
    rows = terms.shape[0] // (n_dp * n_frame * n_row)
    chans = terms.shape[-1]
    blocks = terms.reshape(n_dp * n_frame, n_row * rows, chans)
    blocks = a2a_sum(blocks, ("dp", "frame"))
    return halving_sum(blocks.reshape(n_row, rows, chans), "row")


def width_taps(a, reverse):
    zero = jnp.zeros_like(a[:, :, :1])
    left = jnp.concatenate([zero, a[:, :, :-1]], axis=2)
    right = jnp.concatenate([a[:, :, 1:], zero], axis=2)
    parts = [right, a, left] if reverse else [left, a, right]
    return jnp.concatenate(parts, axis=-1)


def frame_taps(ext, frames, later):
    if later:
        parts = [ext[:, k : k + frames] for k in range(3)]
    else:
        parts = [ext[:, 2 - k : 2 - k + frames] for k in range(3)]
    return jnp.concatenate(parts, axis=-1)


def on_device(clip_input, cotangent, spatial_weight, temporal_weight):
    x = jnp.transpose(clip_input[0], (1, 0, 2, 3))
    g = jnp.transpose(cotangent[0], (1, 0, 2, 3))
    rows, frames, cols, chans = x.shape
    cells = (
        lax.axis_size("dp") * frames * lax.axis_size("frame") * rows * lax.axis_size("row") * cols
    )
    scale = 1.0 / math.sqrt(cells)
    f32 = jnp.float32
    bf16 = jnp.bfloat16

    x_ext = row_halo(x)
    g_next = frame_shift(g[:, :2], forward=False)
    x3 = width_taps(x_ext, reverse=False)
    fwd_weight = spatial_weight.reshape(3, 3 * chans, chans)
    pre = jnp.zeros((rows * frames * cols, chans), f32)
    for i in range(3):
        piece = x3[i : i + rows].reshape(-1, 3 * chans)
        pre = pre + jnp.dot(piece, fwd_weight[i], preferred_element_type=f32)
    pre = pre.reshape(x.shape)
    act = jax.nn.silu(pre).astype(bf16)
    act_prev = frame_shift(act[:, frames - 2 :], forward=True)
    act3 = frame_taps(jnp.concatenate([act_prev, act], axis=1), frames, later=False)
    g3 = frame_taps(jnp.concatenate([g, g_next], axis=1), frames, later=True)
    act3_flat = act3.reshape(-1, 3 * chans)
    g_flat = g.reshape(-1, chans)

    mixed = jnp.dot(act3_flat, temporal_weight.reshape(3 * chans, chans), preferred_element_type=f32)
    back_temporal = jnp.transpose(temporal_weight, (0, 2, 1)).reshape(3 * chans, chans)
    act_grad = jnp.dot(g3.reshape(-1, 3 * chans), back_temporal, preferred_element_type=f32)
    temporal_grad = lax.dot_general(
        act3_flat, g_flat, (((0,), (0,)), ((), ())), preferred_element_type=f32
    )
    mixed = mixed.astype(bf16).reshape(x.shape)
    act_grad = act_grad.astype(bf16).reshape(x.shape)
    block_output = (x.astype(f32) + mixed.astype(f32)).astype(bf16)

    sigma = jax.nn.sigmoid(pre)
    pre_grad = (act_grad.astype(f32) * sigma * (1.0 + pre * (1.0 - sigma))).astype(bf16)
    pg_flat = pre_grad.reshape(-1, chans)

    spatial_list = []
    for i in range(3):
        piece = x3[i : i + rows].reshape(-1, 3 * chans)
        spatial_list.append(
            lax.dot_general(piece, pg_flat, (((0,), (0,)), ((), ())), preferred_element_type=f32)
        )
    pg3 = width_taps(row_halo(pre_grad), reverse=True)
    back_weight = jnp.transpose(spatial_weight, (0, 1, 3, 2)).reshape(3, 3 * chans, chans)
    back = g.astype(f32).reshape(-1, chans)
    for i in range(3):
        piece = pg3[2 - i : 2 - i + rows].reshape(-1, 3 * chans)
        back = back + jnp.dot(piece, back_weight[i], preferred_element_type=f32)
    input_grad = back.astype(bf16).reshape(x.shape)

    partial_terms = jnp.concatenate(spatial_list + [temporal_grad], axis=0)
    summed = staged_scatter(partial_terms)
    block_output = jnp.transpose(block_output, (1, 0, 2, 3))
    input_grad = jnp.transpose(input_grad, (1, 0, 2, 3))
    return (block_output[None], input_grad[None], summed * scale)


def solution(mesh):
    placed = (P("dp", "frame", "row", None, None), P("dp", "frame", "row", None, None), P(), P())
    return jax.shard_map(
        on_device,
        mesh=mesh,
        in_specs=placed,
        out_specs=(
            P("dp", "frame", "row", None, None),
            P("dp", "frame", "row", None, None),
            P(("dp", "frame", "row"), None),
        ),
        check_vma=False,
    )
```
